32 devices in a mesh: grp: 4 (over z), node: 8 (over y, x, core).
Axes of the slice: x: 2, y: 2, z: 4, core: 2. Of those that a mesh axis runs over, the one named last changes fastest.
Arguments:
- params: bfloat16 [4, 14336, 4096], P('grp', 'node'), may hold values from -6 to 6
- momentum: bfloat16 [4, 14336, 4096], P('grp', 'node'), may hold values from -0.125 to 0.125
- hidden: bfloat16 [4, 1024, 14336], P('grp', 'node'), may hold values from -6 to 6
- cotangent: bfloat16 [4, 1024, 4096], P('grp', 'node'), may hold values from -6 to 6
- push_weight: float32 [4], P('grp'), may hold values from 0.5 to 2
- offsets: int32 [64], replicated, may hold values from 1 to 3
- step: int32 [1], replicated, may hold values from 0 to 63
Outputs:
- mixed: bfloat16 [4, 14336, 4096], P('grp', 'node')
- new_weight: float32 [4], P('grp')
The draws below stay inside these ranges and needn't reach their ends.
All inputs are finite; a program needn't handle non-finite values.
Results may differ from the reference program's by a relative error of at most 0.005.
Values may be sent and summed in bfloat16 or wider, within the bound.
No kernel may reach another device: no remote copies, remote signals or barrier semaphores. Data moves between devices by JAX's collectives and lax.ppermute only.
A program may use at most 192 MiB of HBM per device.

```python
import math
import jax
import jax.numpy as jnp
from jax import lax

D = 4096
FF = 14336
HISTORY = 64
TOK_GRP = 1024
N_GRP = 4


def set_ends(drawn, rng, smallest, largest):
    longest = drawn.shape.index(max(drawn.shape))
    spots = []
    for shift in (0, 1):
        where = [jax.random.randint(jax.random.fold_in(rng, axis), (), 0, length) for axis, length in enumerate(drawn.shape)]
        where[longest] = (where[longest] + shift) % drawn.shape[longest]
        spots.append(tuple(where))
    return drawn.at[spots[0]].set(smallest).at[spots[1]].set(largest)


def levels(stream_key, shape, cuts, low, largest):
    factor_of, own = 1.0, jax.random.fold_in(stream_key, 6)
    for dim, blocks in cuts:
        heights = jnp.exp(jax.random.uniform(jax.random.fold_in(own, dim), (blocks,), jnp.float32, low / len(cuts), largest / len(cuts)))
        factor_of = factor_of * jnp.repeat(heights, shape[dim] // blocks).reshape([-1 if axis == dim else 1 for axis in range(len(shape))])
    return factor_of


def bell_draw(stream_key, dims, scale, limit, cuts=(), held_as=jnp.bfloat16):
    drawn = jax.random.normal(stream_key, dims, jnp.float32) * scale
    if len(cuts) > 0:
        drawn = levels(stream_key, dims, cuts, -0.22, 0.18) * drawn
    return jnp.clip(drawn, min=-limit, max=limit).astype(held_as)


def setup_inputs(seed: int = 0) -> dict:
    key_list = jax.random.split(jax.random.key(seed), 8)
    params = bell_draw(key_list[0], (N_GRP, FF, D), 1.0, 6.0, ((0, 4), (1, 8)))
    momentum = bell_draw(key_list[1], (N_GRP, FF, D), 0.02, 0.125, ((0, 4), (1, 8)))
    hidden = bell_draw(key_list[2], (N_GRP, TOK_GRP, FF), 1.0, 6.0, ((0, 4), (1, 8)))
    cotangent = bell_draw(key_list[3], (N_GRP, TOK_GRP, D), 1.0, 6.0, ((0, 4), (1, 8)))
    push_weight = jnp.clip(jnp.exp(math.log(2.0) - 1.3862944 * jax.random.uniform(key_list[4], (N_GRP,), jnp.float32) ** levels(key_list[4], (N_GRP,), ((0, 4),), -0.2, 0.2)), 0.5, 2.0)
    offsets = set_ends(jax.random.randint(key_list[5], (HISTORY,), 1, N_GRP), jax.random.fold_in(key_list[5], 1), 1, N_GRP - 1).astype(jnp.int32)
    step = jax.random.randint(key_list[6], (1,), 0, HISTORY).astype(jnp.int32)
    return {"params": params, "momentum": momentum, "hidden": hidden, "cotangent": cotangent, "push_weight": push_weight, "offsets": offsets, "step": step}


base_rate = 40.0
moment_decay = 0.9
keep_share = 0.5
back_share = 0.3
front_share = 0.2


def reference(params, momentum, hidden, cotangent, push_weight, offsets, step):
    position = step[0]
    offset = offsets[position].astype(jnp.int32)
    rate = base_rate * (1.0 - 0.5 * position.astype(jnp.float32) / HISTORY)
    group_ids = jnp.arange(N_GRP, dtype=jnp.int32)

    def half_step(group):
        grad = jnp.dot(hidden[group].T, cotangent[group], preferred_element_type=jnp.float32) / TOK_GRP
        renewed = moment_decay * momentum[group].astype(jnp.float32) + grad
        return (params[group].astype(jnp.float32) - rate * renewed).astype(jnp.bfloat16)

    halfway = lax.map(half_step, group_ids)

    def mix_one(group):
        back = ((group - offset) % N_GRP).astype(jnp.int32)
        front = ((group + offset) % N_GRP).astype(jnp.int32)
        total = keep_share * halfway[group].astype(jnp.float32) + back_share * halfway[back].astype(jnp.float32) + front_share * halfway[front].astype(jnp.float32)
        return total.astype(jnp.bfloat16)

    mixed = lax.map(mix_one, group_ids)
    back_all = ((group_ids - offset) % N_GRP).astype(jnp.int32)
    front_all = ((group_ids + offset) % N_GRP).astype(jnp.int32)
    new_weight = keep_share * push_weight + back_share * push_weight[back_all] + front_share * push_weight[front_all]
    return mixed, new_weight
```

```python
import jax
import jax.numpy as jnp
from jax import lax
from jax.sharding import PartitionSpec as P

base_rate = 40.0
moment_decay = 0.9
keep_share = 0.5
back_share = 0.3
front_share = 0.2
tokens_axis = (((0,), (0,)), ((), ()))
target_chunks = 8


def shifted(value, axis, steps):
    count = lax.axis_size(axis)
    pairs = [(source, (source + steps) % count) for source in range(count)]
    return lax.ppermute(value, axis, pairs)


def chunk_count(rows):
    for count in range(target_chunks, 0, -1):
        if rows % count == 0 and (rows // count) % 16 == 0:
            return count
    return 1


def pipeline(amount, groups, chunks, params, momentum, acts, cots, push_weight, rate):
    tok_group = cots.shape[0]
    size = params.shape[1] // chunks
    paired = (2 * amount) % groups == 0
    outs = []
    for k in range(chunks):
        cols = lax.all_to_all(acts[:, :, k, :], "node", split_axis=1, concat_axis=0, tiled=True)
        cols = cols.reshape(tok_group, size)
        grad = lax.dot_general(cols, cots, tokens_axis, preferred_element_type=jnp.float32)
        grad = grad / tok_group
        rows = slice(k * size, (k + 1) * size)
        renewed = moment_decay * momentum[0, rows].astype(jnp.float32) + grad
        half = (params[0, rows].astype(jnp.float32) - rate * renewed).astype(jnp.bfloat16)
        behind = shifted(half, "grp", amount)
        ahead = behind if paired else shifted(half, "grp", groups - amount)
        total = (
            keep_share * half.astype(jnp.float32)
            + back_share * behind.astype(jnp.float32)
            + front_share * ahead.astype(jnp.float32)
        )
        outs.append(total.astype(jnp.bfloat16))
    mixed = jnp.concatenate(outs, axis=0)
    weight_behind = shifted(push_weight, "grp", amount)
    weight_ahead = shifted(push_weight, "grp", groups - amount)
    new_weight = keep_share * push_weight + back_share * weight_behind + front_share * weight_ahead
    return mixed[None], new_weight


def per_device(params, momentum, hidden, cotangent, push_weight, offsets, step):
    groups = lax.axis_size("grp")
    nodes = lax.axis_size("node")
    position = step[0]
    offset = offsets[position]
    rate = base_rate * (1.0 - 0.5 * position.astype(jnp.float32) / offsets.shape[0])
    cots = lax.all_gather(cotangent[0], "node", axis=0, tiled=True)
    chunks = chunk_count(params.shape[1])
    size = params.shape[1] // chunks
    acts = hidden[0].reshape(hidden.shape[1], nodes, chunks, size)
    branches = [
        (lambda *a, amount=amount: pipeline(amount, groups, chunks, *a))
        for amount in range(1, groups)
    ]
    return lax.switch(offset - 1, branches, params, momentum, acts, cots, push_weight, rate)


def solution(mesh):
    in_specs = (
        P("grp", "node", None),
        P("grp", "node", None),
        P("grp", "node", None),
        P("grp", "node", None),
        P("grp"),
        P(),
        P(),
    )
    out_specs = (P("grp", "node", None), P("grp"))
    return jax.shard_map(
        per_device, mesh=mesh, in_specs=in_specs, out_specs=out_specs, check_vma=False
    )
```

```python
import jax
import jax.numpy as jnp
from jax import lax
from jax.sharding import PartitionSpec as P

base_rate = 40.0
moment_decay = 0.9
keep_share = 0.5
back_share = 0.3
front_share = 0.2
tokens_axis = (((0,), (0,)), ((), ()))
row_blocks = 4
col_blocks = 4


def shifted(value, axis, steps):
    count = lax.axis_size(axis)
    pairs = [(source, (source + steps) % count) for source in range(count)]
    return lax.ppermute(value, axis, pairs)


def block_count(length, target, quantum):
    for count in range(target, 0, -1):
        if length % count == 0 and (length // count) % quantum == 0:
            return count
    return 1


def pipeline(amount, groups, params, momentum, acts, cotangent, push_weight, rate, direct):
    n_rows, row_size = acts.shape[2], acts.shape[3]
    width = cotangent.shape[1]
    n_cols = block_count(width, col_blocks, 128)
    col_size = width // n_cols
    paired = (2 * amount) % groups == 0
    w_minus = jnp.where(direct, back_share, front_share).astype(jnp.float32)
    w_plus = jnp.where(direct, front_share, back_share).astype(jnp.float32)
    cots = [None] * n_cols
    row_parts = []
    for a in range(n_rows):
        col_parts = []
        cols = lax.all_to_all(acts[:, :, a, :], "node", split_axis=1, concat_axis=0, tiled=True)
        cols = cols.reshape(-1, row_size)
        tok_group = cols.shape[0]
        rows = slice(a * row_size, (a + 1) * row_size)
        for b in range(n_cols):
            span = slice(b * col_size, (b + 1) * col_size)
            if cots[b] is None:
                cots[b] = lax.all_gather(cotangent[:, span], "node", axis=0, tiled=True)
            grad = lax.dot_general(cols, cots[b], tokens_axis, preferred_element_type=jnp.float32)
            grad = grad / tok_group
            renewed = moment_decay * momentum[0, rows, span].astype(jnp.float32) + grad
            half = (params[0, rows, span].astype(jnp.float32) - rate * renewed).astype(jnp.bfloat16)
            minus = shifted(half, "grp", amount)
            if paired:
                peers = (back_share * minus.astype(jnp.float32)) + front_share * minus.astype(jnp.float32)
            else:
                plus = shifted(half, "grp", groups - amount)
                peers = w_minus * minus.astype(jnp.float32) + w_plus * plus.astype(jnp.float32)
            total = keep_share * half.astype(jnp.float32) + peers
            col_parts.append(total.astype(jnp.bfloat16))
        row_parts.append(jnp.concatenate(col_parts, axis=1))
    mixed = jnp.concatenate(row_parts, axis=0)
    weight_minus = shifted(push_weight, "grp", amount)
    weight_plus = shifted(push_weight, "grp", groups - amount)
    new_weight = keep_share * push_weight + w_minus * weight_minus + w_plus * weight_plus
    return mixed[None], new_weight


def per_device(params, momentum, hidden, cotangent, push_weight, offsets, step):
    groups = lax.axis_size("grp")
    nodes = lax.axis_size("node")
    position = step[0]
    offset = offsets[position]
    rate = base_rate * (1.0 - 0.5 * position.astype(jnp.float32) / offsets.shape[0])
    rows = params.shape[1]
    n_rows = block_count(rows, row_blocks, 16)
    acts = hidden[0].reshape(hidden.shape[1], nodes, n_rows, rows // n_rows)
    amounts = list(range(1, groups // 2 + 1))
    direct = offset <= groups // 2
    index = jnp.where(direct, offset, groups - offset) - 1
    branches = [
        (lambda *a, amount=amount: pipeline(amount, groups, *a))
        for amount in amounts
    ]
    return lax.switch(
        index, branches, params, momentum, acts, cotangent[0], push_weight, rate, direct
    )


def solution(mesh):
    in_specs = (
        P("grp", "node", None),
        P("grp", "node", None),
        P("grp", "node", None),
        P("grp", "node", None),
        P("grp"),
        P(),
        P(),
    )
    out_specs = (P("grp", "node", None), P("grp"))
    return jax.shard_map(
        per_device, mesh=mesh, in_specs=in_specs, out_specs=out_specs, check_vma=False
    )
```

```python
import jax
import jax.numpy as jnp
from jax import lax
from jax.sharding import PartitionSpec as P

base_rate = 40.0
moment_decay = 0.9
keep_share = 0.5
back_share = 0.3
front_share = 0.2
tokens_axis = (((0,), (0,)), ((), ()))
col_blocks = 4


def shifted(value, axis, steps):
    count = lax.axis_size(axis)
    pairs = [(source, (source + steps) % count) for source in range(count)]
    return lax.ppermute(value, axis, pairs)


def block_count(length, target, quantum):
    for count in range(target, 0, -1):
        if length % count == 0 and (length // count) % quantum == 0:
            return count
    return 1


def row_sizes(rows, quantum=16):
    first = 128 if rows >= 512 and rows % quantum == 0 else rows
    rest = rows - first
    if rest == 0:
        return [first]
    units = rest // quantum
    parts = [units // 3 + (1 if i < units % 3 else 0) for i in range(3)]
    return [first] + [p * quantum for p in parts if p > 0]


def pipeline(amount, groups, params, momentum, hidden, cotangent, push_weight, rate, direct):
    nodes = lax.axis_size("node")
    rows_total = params.shape[1]
    acts = hidden.reshape(hidden.shape[0], nodes, rows_total)
    width = cotangent.shape[1]
    n_cols = block_count(width, col_blocks, 128)
    col_size = width // n_cols
    paired = (2 * amount) % groups == 0
    w_minus = jnp.where(direct, back_share, front_share).astype(jnp.float32)
    w_plus = jnp.where(direct, front_share, back_share).astype(jnp.float32)
    cots = [
        lax.all_gather(cotangent[:, b * col_size:(b + 1) * col_size], "node", axis=0, tiled=True)
        for b in range(n_cols)
    ]
    mixed = jnp.zeros(params.shape[1:], jnp.bfloat16)
    start = 0
    last = None
    for size in row_sizes(rows_total):
        piece = acts[:, :, start:start + size]
        if last is not None:
            piece, last = lax.optimization_barrier((piece, last))
        cols = lax.all_to_all(piece, "node", split_axis=1, concat_axis=0, tiled=True)
        cols = cols.reshape(-1, size)
        tok_group = cols.shape[0]
        rows = slice(start, start + size)
        for b in range(n_cols):
            span = slice(b * col_size, (b + 1) * col_size)
            grad = lax.dot_general(cols, cots[b], tokens_axis, preferred_element_type=jnp.float32)
            grad = grad / tok_group
            renewed = moment_decay * momentum[0, rows, span].astype(jnp.float32) + grad
            half = (params[0, rows, span].astype(jnp.float32) - rate * renewed).astype(jnp.bfloat16)
            if b == 0:
                last = half
            minus = shifted(half, "grp", amount)
            if paired:
                peers = (back_share * minus.astype(jnp.float32)) + front_share * minus.astype(jnp.float32)
            else:
                plus = shifted(half, "grp", groups - amount)
                peers = w_minus * minus.astype(jnp.float32) + w_plus * plus.astype(jnp.float32)
            total = keep_share * half.astype(jnp.float32) + peers
            mixed = lax.dynamic_update_slice(mixed, total.astype(jnp.bfloat16), (start, b * col_size))
        start += size
    weight_minus = shifted(push_weight, "grp", amount)
    weight_plus = shifted(push_weight, "grp", groups - amount)
    new_weight = keep_share * push_weight + w_minus * weight_minus + w_plus * weight_plus
    return mixed[None], new_weight


def per_device(params, momentum, hidden, cotangent, push_weight, offsets, step):
    groups = lax.axis_size("grp")
    position = step[0]
    offset = offsets[position]
    rate = base_rate * (1.0 - 0.5 * position.astype(jnp.float32) / offsets.shape[0])
    amounts = list(range(1, groups // 2 + 1))
    direct = offset <= groups // 2
    index = jnp.where(direct, offset, groups - offset) - 1
    branches = [
        (lambda *a, amount=amount: pipeline(amount, groups, *a))
        for amount in amounts
    ]
    return lax.switch(
        index, branches, params, momentum, hidden[0], cotangent[0], push_weight, rate, direct
    )


def solution(mesh):
    in_specs = (
        P("grp", "node", None),
        P("grp", "node", None),
        P("grp", "node", None),
        P("grp", "node", None),
        P("grp"),
        P(),
        P(),
    )
    out_specs = (P("grp", "node", None), P("grp"))
    return jax.shard_map(
        per_device, mesh=mesh, in_specs=in_specs, out_specs=out_specs, check_vma=False
    )
```

```python
import jax
import jax.numpy as jnp
from jax import lax
from jax.sharding import PartitionSpec as P

base_rate = 40.0
moment_decay = 0.9
keep_share = 0.5
back_share = 0.3
front_share = 0.2
tokens_axis = (((0,), (0,)), ((), ()))
col_blocks = 4


def shifted(value, axis, steps):
    count = lax.axis_size(axis)
    pairs = [(source, (source + steps) % count) for source in range(count)]
    return lax.ppermute(value, axis, pairs)


def block_count(length, target, quantum):
    for count in range(target, 0, -1):
        if length % count == 0 and (length // count) % quantum == 0:
            return count
    return 1


def row_sizes(rows, quantum=16):
    sizes, size, left = [], 128, rows
    while left > 0:
        take = left if (left - size < size or size % quantum) else size
        sizes.append(take)
        left -= take
        size *= 2
    return sizes


def pipeline(amount, groups, params, momentum, hidden, cotangent, push_weight, rate, direct):
    nodes = lax.axis_size("node")
    rows_total = params.shape[1]
    acts = hidden.reshape(hidden.shape[0], nodes, rows_total)
    width = cotangent.shape[1]
    n_cols = block_count(width, col_blocks, 128)
    col_size = width // n_cols
    paired = (2 * amount) % groups == 0
    w_minus = jnp.where(direct, back_share, front_share).astype(jnp.float32)
    w_plus = jnp.where(direct, front_share, back_share).astype(jnp.float32)
    cots = [
        lax.all_gather(cotangent[:, b * col_size:(b + 1) * col_size], "node", axis=0, tiled=True)
        for b in range(n_cols)
    ]
    mixed = jnp.zeros(params.shape[1:], jnp.bfloat16)
    sizes = row_sizes(rows_total)
    starts = [sum(sizes[:i]) for i in range(len(sizes))]
    columns = [None] * len(sizes)
    last = None
    for b in range(n_cols):
        span = slice(b * col_size, (b + 1) * col_size)
        for a, (start, size) in enumerate(zip(starts, sizes)):
            if columns[a] is None:
                piece = acts[:, :, start:start + size]
                if last is not None:
                    piece, last = lax.optimization_barrier((piece, last))
                cols = lax.all_to_all(piece, "node", split_axis=1, concat_axis=0, tiled=True)
                columns[a] = cols.reshape(-1, size)
            cols = columns[a]
            tok_group = cols.shape[0]
            rows = slice(start, start + size)
            grad = lax.dot_general(cols, cots[b], tokens_axis, preferred_element_type=jnp.float32)
            grad = grad / tok_group
            renewed = moment_decay * momentum[0, rows, span].astype(jnp.float32) + grad
            half = (params[0, rows, span].astype(jnp.float32) - rate * renewed).astype(jnp.bfloat16)
            last = half
            minus = shifted(half, "grp", amount)
            if paired:
                peers = (back_share * minus.astype(jnp.float32)) + front_share * minus.astype(jnp.float32)
            else:
                plus = shifted(half, "grp", groups - amount)
                peers = w_minus * minus.astype(jnp.float32) + w_plus * plus.astype(jnp.float32)
            total = keep_share * half.astype(jnp.float32) + peers
            mixed = lax.dynamic_update_slice(mixed, total.astype(jnp.bfloat16), (start, b * col_size))
    weight_minus = shifted(push_weight, "grp", amount)
    weight_plus = shifted(push_weight, "grp", groups - amount)
    new_weight = keep_share * push_weight + w_minus * weight_minus + w_plus * weight_plus
    return mixed[None], new_weight


def per_device(params, momentum, hidden, cotangent, push_weight, offsets, step):
    groups = lax.axis_size("grp")
    position = step[0]
    offset = offsets[position]
    rate = base_rate * (1.0 - 0.5 * position.astype(jnp.float32) / offsets.shape[0])
    amounts = list(range(1, groups // 2 + 1))
    direct = offset <= groups // 2
    index = jnp.where(direct, offset, groups - offset) - 1
    branches = [
        (lambda *a, amount=amount: pipeline(amount, groups, *a))
        for amount in amounts
    ]
    return lax.switch(
        index, branches, params, momentum, hidden[0], cotangent[0], push_weight, rate, direct
    )


def solution(mesh):
    in_specs = (
        P("grp", "node", None),
        P("grp", "node", None),
        P("grp", "node", None),
        P("grp", "node", None),
        P("grp"),
        P(),
        P(),
    )
    out_specs = (P("grp", "node", None), P("grp"))
    return jax.shard_map(
        per_device, mesh=mesh, in_specs=in_specs, out_specs=out_specs, check_vma=False
    )
```

```python
import jax
import jax.numpy as jnp
from jax import lax
from jax.sharding import PartitionSpec as P

base_rate = 40.0
moment_decay = 0.9
keep_share = 0.5
back_share = 0.3
front_share = 0.2
tokens_axis = (((0,), (0,)), ((), ()))
col_blocks = 4


def shifted(value, axis, steps):
    count = lax.axis_size(axis)
    pairs = [(source, (source + steps) % count) for source in range(count)]
    return lax.ppermute(value, axis, pairs)


def block_count(length, target, quantum):
    for count in range(target, 0, -1):
        if length % count == 0 and (length // count) % quantum == 0:
            return count
    return 1


def row_sizes(rows, quantum=16):
    sizes, size, left = [], 128, rows
    while left > 0:
        take = left if (left - size < size or size % quantum) else size
        sizes.append(take)
        left -= take
        size *= 2
    return sizes


def pipeline(amount, groups, params, momentum, hidden, cotangent, push_weight, rate, direct):
    nodes = lax.axis_size("node")
    rows_total = params.shape[1]
    acts = hidden.reshape(hidden.shape[0], nodes, rows_total)
    width = cotangent.shape[1]
    n_cols = block_count(width, col_blocks, 128)
    col_size = width // n_cols
    paired = (2 * amount) % groups == 0
    w_minus = jnp.where(direct, back_share, front_share).astype(jnp.float32)
    w_plus = jnp.where(direct, front_share, back_share).astype(jnp.float32)
    cots = [
        lax.all_gather(cotangent[:, b * col_size:(b + 1) * col_size], "node", axis=0, tiled=True)
        for b in range(n_cols)
    ]
    mixed = jnp.zeros(params.shape[1:], jnp.bfloat16)
    sizes = row_sizes(rows_total)
    starts = [sum(sizes[:i]) for i in range(len(sizes))]
    columns = [None] * len(sizes)
    last = None
    for b in range(n_cols):
        span = slice(b * col_size, (b + 1) * col_size)
        for a, (start, size) in enumerate(zip(starts, sizes)):
            if columns[a] is None:
                piece = acts[:, :, start:start + size]
                if last is not None:
                    piece, last = lax.optimization_barrier((piece, last))
                cols = lax.all_to_all(piece, "node", split_axis=1, concat_axis=0, tiled=True)
                columns[a] = cols.reshape(-1, size)
            cols, cot = columns[a], cots[b]
            if last is not None:
                cols, cot, last = lax.optimization_barrier((cols, cot, last))
            tok_group = cols.shape[0]
            rows = slice(start, start + size)
            grad = lax.dot_general(cols, cot, tokens_axis, preferred_element_type=jnp.float32)
            grad = grad / tok_group
            renewed = moment_decay * momentum[0, rows, span].astype(jnp.float32) + grad
            half = (params[0, rows, span].astype(jnp.float32) - rate * renewed).astype(jnp.bfloat16)
            last = half
            minus = shifted(half, "grp", amount)
            if paired:
                peers = (back_share * minus.astype(jnp.float32)) + front_share * minus.astype(jnp.float32)
            else:
                plus = shifted(half, "grp", groups - amount)
                peers = w_minus * minus.astype(jnp.float32) + w_plus * plus.astype(jnp.float32)
            total = keep_share * half.astype(jnp.float32) + peers
            mixed = lax.dynamic_update_slice(mixed, total.astype(jnp.bfloat16), (start, b * col_size))
    weight_minus = shifted(push_weight, "grp", amount)
    weight_plus = shifted(push_weight, "grp", groups - amount)
    new_weight = keep_share * push_weight + w_minus * weight_minus + w_plus * weight_plus
    return mixed[None], new_weight


def per_device(params, momentum, hidden, cotangent, push_weight, offsets, step):
    groups = lax.axis_size("grp")
    position = step[0]
    offset = offsets[position]
    rate = base_rate * (1.0 - 0.5 * position.astype(jnp.float32) / offsets.shape[0])
    amounts = list(range(1, groups // 2 + 1))
    direct = offset <= groups // 2
    index = jnp.where(direct, offset, groups - offset) - 1
    branches = [
        (lambda *a, amount=amount: pipeline(amount, groups, *a))
        for amount in amounts
    ]
    return lax.switch(
        index, branches, params, momentum, hidden[0], cotangent[0], push_weight, rate, direct
    )


def solution(mesh):
    in_specs = (
        P("grp", "node", None),
        P("grp", "node", None),
        P("grp", "node", None),
        P("grp", "node", None),
        P("grp"),
        P(),
        P(),
    )
    out_specs = (P("grp", "node", None), P("grp"))
    return jax.shard_map(
        per_device, mesh=mesh, in_specs=in_specs, out_specs=out_specs, check_vma=False
    )
```

```python
import jax
import jax.numpy as jnp
from jax import lax
from jax.sharding import PartitionSpec as P

base_rate = 40.0
moment_decay = 0.9
keep_share = 0.5
back_share = 0.3
front_share = 0.2
rows_by_tokens = (((1,), (0,)), ((), ()))
col_blocks = 4


def shifted(value, axis, steps):
    count = lax.axis_size(axis)
    pairs = [(source, (source + steps) % count) for source in range(count)]
    return lax.ppermute(value, axis, pairs)


def block_count(length, target, quantum):
    for count in range(target, 0, -1):
        if length % count == 0 and (length // count) % quantum == 0:
            return count
    return 1


def row_sizes(rows, quantum=16):
    sizes, size, left = [], 128, rows
    while left > 0:
        take = left if (left - size < size or size % quantum) else size
        sizes.append(take)
        left -= take
        size *= 2
    return sizes


def pipeline(amount, groups, params, momentum, hidden, cotangent, push_weight, rate, direct):
    nodes = lax.axis_size("node")
    rows_total = params.shape[1]
    acts = hidden.reshape(hidden.shape[0], nodes, rows_total)
    width = cotangent.shape[1]
    n_cols = block_count(width, col_blocks, 128)
    col_size = width // n_cols
    paired = (2 * amount) % groups == 0
    w_minus = jnp.where(direct, back_share, front_share).astype(jnp.float32)
    w_plus = jnp.where(direct, front_share, back_share).astype(jnp.float32)
    cots = [
        lax.all_gather(cotangent[:, b * col_size:(b + 1) * col_size], "node", axis=0, tiled=True)
        for b in range(n_cols)
    ]
    mixed = jnp.zeros(params.shape[1:], jnp.bfloat16)
    sizes = row_sizes(rows_total)
    starts = [sum(sizes[:i]) for i in range(len(sizes))]
    columns = [None] * len(sizes)
    weight_sent = None
    last = None
    for b in range(n_cols):
        span = slice(b * col_size, (b + 1) * col_size)
        for a, (start, size) in enumerate(zip(starts, sizes)):
            if columns[a] is None:
                piece = acts[:, :, start:start + size]
                if last is not None:
                    piece, last = lax.optimization_barrier((piece, last))
                cols = lax.all_to_all(piece, "node", split_axis=1, concat_axis=0, tiled=True)
                columns[a] = cols.reshape(-1, size).T
            cols, cot = columns[a], cots[b]
            if last is not None:
                cols, cot, last = lax.optimization_barrier((cols, cot, last))
            tok_group = cols.shape[1]
            rows = slice(start, start + size)
            grad = lax.dot_general(cols, cot, rows_by_tokens, preferred_element_type=jnp.float32)
            grad = grad / tok_group
            renewed = moment_decay * momentum[0, rows, span].astype(jnp.float32) + grad
            half = (params[0, rows, span].astype(jnp.float32) - rate * renewed).astype(jnp.bfloat16)
            last = half
            if weight_sent is None and b == 0 and a == len(sizes) - 1:
                weight, last = lax.optimization_barrier((push_weight, last))
                weight_sent = (shifted(weight, "grp", amount), shifted(weight, "grp", groups - amount))
            minus = shifted(half, "grp", amount)
            if paired:
                peers = (back_share * minus.astype(jnp.float32)) + front_share * minus.astype(jnp.float32)
            else:
                plus = shifted(half, "grp", groups - amount)
                peers = w_minus * minus.astype(jnp.float32) + w_plus * plus.astype(jnp.float32)
            total = keep_share * half.astype(jnp.float32) + peers
            mixed = lax.dynamic_update_slice(mixed, total.astype(jnp.bfloat16), (start, b * col_size))
    weight_minus, weight_plus = weight_sent
    new_weight = keep_share * push_weight + w_minus * weight_minus + w_plus * weight_plus
    return mixed[None], new_weight


def per_device(params, momentum, hidden, cotangent, push_weight, offsets, step):
    groups = lax.axis_size("grp")
    position = step[0]
    offset = offsets[position]
    rate = base_rate * (1.0 - 0.5 * position.astype(jnp.float32) / offsets.shape[0])
    amounts = list(range(1, groups // 2 + 1))
    direct = offset <= groups // 2
    index = jnp.where(direct, offset, groups - offset) - 1
    branches = [
        (lambda *a, amount=amount: pipeline(amount, groups, *a))
        for amount in amounts
    ]
    return lax.switch(
        index, branches, params, momentum, hidden[0], cotangent[0], push_weight, rate, direct
    )


def solution(mesh):
    in_specs = (
        P("grp", "node", None),
        P("grp", "node", None),
        P("grp", "node", None),
        P("grp", "node", None),
        P("grp"),
        P(),
        P(),
    )
    out_specs = (P("grp", "node", None), P("grp"))
    return jax.shard_map(
        per_device, mesh=mesh, in_specs=in_specs, out_specs=out_specs, check_vma=False
    )
```

```python
import jax
import jax.numpy as jnp
from jax import lax
from jax.sharding import PartitionSpec as P

base_rate = 40.0
moment_decay = 0.9
keep_share = 0.5
back_share = 0.3
front_share = 0.2
rows_by_tokens = (((1,), (0,)), ((), ()))
col_blocks = 4


def shifted(value, axis, steps):
    count = lax.axis_size(axis)
    pairs = [(source, (source + steps) % count) for source in range(count)]
    return lax.ppermute(value, axis, pairs)


def block_count(length, target, quantum):
    for count in range(target, 0, -1):
        if length % count == 0 and (length // count) % quantum == 0:
            return count
    return 1


def row_sizes(rows, quantum=16):
    sizes, size, left = [], 128, rows
    while left > 0:
        take = left if (left - size < size or size % quantum) else size
        sizes.append(take)
        left -= take
        size *= 2
    return sizes


def pipeline(amount, groups, params, momentum, hidden, cotangent, push_weight, rate, direct):
    nodes = lax.axis_size("node")
    rows_total = params.shape[1]
    acts = hidden.reshape(hidden.shape[0], nodes, rows_total)
    width = cotangent.shape[1]
    n_cols = block_count(width, col_blocks, 128)
    col_size = width // n_cols
    paired = (2 * amount) % groups == 0
    w_minus = jnp.where(direct, back_share, front_share).astype(jnp.float32)
    w_plus = jnp.where(direct, front_share, back_share).astype(jnp.float32)
    cots = [
        lax.all_gather(cotangent[:, b * col_size:(b + 1) * col_size], "node", axis=0, tiled=True)
        for b in range(n_cols)
    ]
    mixed = jnp.zeros(params.shape[1:], jnp.bfloat16)
    sizes = row_sizes(rows_total)
    starts = [sum(sizes[:i]) for i in range(len(sizes))]
    columns = [None] * len(sizes)
    weight_sent = None
    last = None
    for b in range(n_cols):
        span = slice(b * col_size, (b + 1) * col_size)
        for a, (start, size) in enumerate(zip(starts, sizes)):
            if columns[a] is None:
                members = [0, 1][:len(sizes)] if a == 0 else [a]
                width_a = sum(sizes[m] for m in members)
                piece = acts[:, :, start:start + width_a]
                if last is not None:
                    piece, last = lax.optimization_barrier((piece, last))
                cols = lax.all_to_all(piece, "node", split_axis=1, concat_axis=0, tiled=True)
                cols = cols.reshape(-1, width_a).T
                offset_a = 0
                for m in members:
                    columns[m] = cols[offset_a:offset_a + sizes[m]]
                    offset_a += sizes[m]
            cols, cot = columns[a], cots[b]
            if last is not None:
                cols, cot, last = lax.optimization_barrier((cols, cot, last))
            tok_group = cols.shape[1]
            rows = slice(start, start + size)
            grad = lax.dot_general(cols, cot, rows_by_tokens, preferred_element_type=jnp.float32)
            grad = grad / tok_group
            renewed = moment_decay * momentum[0, rows, span].astype(jnp.float32) + grad
            half = (params[0, rows, span].astype(jnp.float32) - rate * renewed).astype(jnp.bfloat16)
            last = half
            if weight_sent is None and b == 0 and a == len(sizes) - 1:
                weight, last = lax.optimization_barrier((push_weight, last))
                weight_sent = (shifted(weight, "grp", amount), shifted(weight, "grp", groups - amount))
            minus = shifted(half, "grp", amount)
            if paired:
                peers = (back_share * minus.astype(jnp.float32)) + front_share * minus.astype(jnp.float32)
            else:
                plus = shifted(half, "grp", groups - amount)
                peers = w_minus * minus.astype(jnp.float32) + w_plus * plus.astype(jnp.float32)
            total = keep_share * half.astype(jnp.float32) + peers
            mixed = lax.dynamic_update_slice(mixed, total.astype(jnp.bfloat16), (start, b * col_size))
    weight_minus, weight_plus = weight_sent
    new_weight = keep_share * push_weight + w_minus * weight_minus + w_plus * weight_plus
    return mixed[None], new_weight


def per_device(params, momentum, hidden, cotangent, push_weight, offsets, step):
    groups = lax.axis_size("grp")
    position = step[0]
    offset = offsets[position]
    rate = base_rate * (1.0 - 0.5 * position.astype(jnp.float32) / offsets.shape[0])
    amounts = list(range(1, groups // 2 + 1))
    direct = offset <= groups // 2
    index = jnp.where(direct, offset, groups - offset) - 1
    branches = [
        (lambda *a, amount=amount: pipeline(amount, groups, *a))
        for amount in amounts
    ]
    return lax.switch(
        index, branches, params, momentum, hidden[0], cotangent[0], push_weight, rate, direct
    )


def solution(mesh):
    in_specs = (
        P("grp", "node", None),
        P("grp", "node", None),
        P("grp", "node", None),
        P("grp", "node", None),
        P("grp"),
        P(),
        P(),
    )
    out_specs = (P("grp", "node", None), P("grp"))
    return jax.shard_map(
        per_device, mesh=mesh, in_specs=in_specs, out_specs=out_specs, check_vma=False
    )
```

```python
import jax
import jax.numpy as jnp
from jax import lax
from jax.sharding import PartitionSpec as P

base_rate = 40.0
moment_decay = 0.9
keep_share = 0.5
back_share = 0.3
front_share = 0.2
rows_by_tokens = (((1,), (0,)), ((), ()))
col_blocks = 4


def shifted(value, axis, steps):
    count = lax.axis_size(axis)
    pairs = [(source, (source + steps) % count) for source in range(count)]
    return lax.ppermute(value, axis, pairs)


def block_count(length, target, quantum):
    for count in range(target, 0, -1):
        if length % count == 0 and (length // count) % quantum == 0:
            return count
    return 1


def row_sizes(rows, quantum=16):
    sizes, size, left = [], 128, rows
    while left > 0:
        take = left if (left - size < size or size % quantum) else size
        sizes.append(take)
        left -= take
        size *= 2
    return sizes


def pipeline(amount, groups, params, momentum, hidden, cotangent, push_weight, rate, direct):
    nodes = lax.axis_size("node")
    rows_total = params.shape[1]
    acts = hidden.reshape(hidden.shape[0], nodes, rows_total)
    width = cotangent.shape[1]
    n_cols = block_count(width, col_blocks, 128)
    col_size = width // n_cols
    paired = (2 * amount) % groups == 0
    w_minus = jnp.where(direct, back_share, front_share).astype(jnp.float32)
    w_plus = jnp.where(direct, front_share, back_share).astype(jnp.float32)
    piece_size = block_count(col_size, col_size // 256 if col_size >= 256 else 1, 128)
    piece_size = col_size // piece_size

    def gathered(b, after):
        block = cotangent[:, b * col_size:(b + 1) * col_size]
        if after is not None:
            block, after = lax.optimization_barrier((block, after))
        parts = [
            lax.all_gather(block[:, lo:lo + piece_size], "node", axis=0, tiled=True)
            for lo in range(0, col_size, piece_size)
        ]
        return jnp.concatenate(parts, axis=1), after

    cots = [None] * n_cols
    cots[0], _ = gathered(0, None)
    mixed = jnp.zeros(params.shape[1:], jnp.bfloat16)
    sizes = row_sizes(rows_total)
    starts = [sum(sizes[:i]) for i in range(len(sizes))]
    columns = [None] * len(sizes)
    weight_sent = None
    last = None
    for b in range(n_cols):
        span = slice(b * col_size, (b + 1) * col_size)
        for a, (start, size) in enumerate(zip(starts, sizes)):
            if columns[a] is None:
                members = [0, 1][:len(sizes)] if a == 0 else [a]
                width_a = sum(sizes[m] for m in members)
                piece = acts[:, :, start:start + width_a]
                if last is not None:
                    piece, last = lax.optimization_barrier((piece, last))
                cols = lax.all_to_all(piece, "node", split_axis=1, concat_axis=0, tiled=True)
                cols = cols.reshape(-1, width_a).T
                offset_a = 0
                for m in members:
                    columns[m] = cols[offset_a:offset_a + sizes[m]]
                    offset_a += sizes[m]
            cols, cot = columns[a], cots[b]
            if last is not None:
                cols, cot, last = lax.optimization_barrier((cols, cot, last))
            tok_group = cols.shape[1]
            rows = slice(start, start + size)
            grad = lax.dot_general(cols, cot, rows_by_tokens, preferred_element_type=jnp.float32)
            grad = grad / tok_group
            renewed = moment_decay * momentum[0, rows, span].astype(jnp.float32) + grad
            half = (params[0, rows, span].astype(jnp.float32) - rate * renewed).astype(jnp.bfloat16)
            last = half
            if b == 0:
                wanted = [a + 1] if a < len(sizes) - 1 else range(a + 1, n_cols)
                for nxt in wanted:
                    if nxt < n_cols and cots[nxt] is None:
                        cots[nxt], last = gathered(nxt, last)
            if weight_sent is None and b == 0 and a == len(sizes) - 1:
                weight, last = lax.optimization_barrier((push_weight, last))
                weight_sent = (shifted(weight, "grp", amount), shifted(weight, "grp", groups - amount))
            minus = shifted(half, "grp", amount)
            if paired:
                peers = (back_share * minus.astype(jnp.float32)) + front_share * minus.astype(jnp.float32)
            else:
                plus = shifted(half, "grp", groups - amount)
                peers = w_minus * minus.astype(jnp.float32) + w_plus * plus.astype(jnp.float32)
            total = keep_share * half.astype(jnp.float32) + peers
            mixed = lax.dynamic_update_slice(mixed, total.astype(jnp.bfloat16), (start, b * col_size))
    weight_minus, weight_plus = weight_sent
    new_weight = keep_share * push_weight + w_minus * weight_minus + w_plus * weight_plus
    return mixed[None], new_weight


def per_device(params, momentum, hidden, cotangent, push_weight, offsets, step):
    groups = lax.axis_size("grp")
    position = step[0]
    offset = offsets[position]
    rate = base_rate * (1.0 - 0.5 * position.astype(jnp.float32) / offsets.shape[0])
    amounts = list(range(1, groups // 2 + 1))
    direct = offset <= groups // 2
    index = jnp.where(direct, offset, groups - offset) - 1
    branches = [
        (lambda *a, amount=amount: pipeline(amount, groups, *a))
        for amount in amounts
    ]
    return lax.switch(
        index, branches, params, momentum, hidden[0], cotangent[0], push_weight, rate, direct
    )


def solution(mesh):
    in_specs = (
        P("grp", "node", None),
        P("grp", "node", None),
        P("grp", "node", None),
        P("grp", "node", None),
        P("grp"),
        P(),
        P(),
    )
    out_specs = (P("grp", "node", None), P("grp"))
    return jax.shard_map(
        per_device, mesh=mesh, in_specs=in_specs, out_specs=out_specs, check_vma=False
    )
```

```python
import jax
import jax.numpy as jnp
from jax import lax
from jax.sharding import PartitionSpec as P

base_rate = 40.0
moment_decay = 0.9
keep_share = 0.5
back_share = 0.3
front_share = 0.2
rows_by_tokens = (((1,), (0,)), ((), ()))


def shifted(value, axis, steps):
    count = lax.axis_size(axis)
    pairs = [(source, (source + steps) % count) for source in range(count)]
    return lax.ppermute(value, axis, pairs)


def block_count(length, target, quantum):
    for count in range(target, 0, -1):
        if length % count == 0 and (length // count) % quantum == 0:
            return count
    return 1


def row_sizes(rows, quantum=16):
    sizes, size, left = [], 128, rows
    while left > 0:
        take = left if (left - size < size or size % quantum) else size
        sizes.append(take)
        left -= take
        if len(sizes) > 1:
            size *= 4 if len(sizes) == 2 else 2
    return sizes


def column_sizes(width):
    first = min(1024, width // 4)
    if first % 128 or first == 0:
        return [width]
    return [first, width - first]


def pipeline(amount, groups, params, momentum, hidden, cotangent, push_weight, rate, direct):
    nodes = lax.axis_size("node")
    rows_total = params.shape[1]
    acts = hidden.reshape(hidden.shape[0], nodes, rows_total)
    width = cotangent.shape[1]
    col_sizes = column_sizes(width)
    n_cols = len(col_sizes)
    col_starts = [sum(col_sizes[:i]) for i in range(n_cols)]
    paired = (2 * amount) % groups == 0
    w_minus = jnp.where(direct, back_share, front_share).astype(jnp.float32)
    w_plus = jnp.where(direct, front_share, back_share).astype(jnp.float32)
    cots = [
        lax.all_gather(cotangent[:, lo:lo + size], "node", axis=0, tiled=True)
        for lo, size in zip(col_starts, col_sizes)
    ]
    mixed = jnp.zeros(params.shape[1:], jnp.bfloat16)
    sizes = row_sizes(rows_total)
    starts = [sum(sizes[:i]) for i in range(len(sizes))]
    columns = [None] * len(sizes)
    weight_sent = None
    last = None
    for b in range(n_cols):
        span = slice(col_starts[b], col_starts[b] + col_sizes[b])
        for a, (start, size) in enumerate(zip(starts, sizes)):
            if columns[a] is None:
                members = [0, 1][:len(sizes)] if a == 0 else [a]
                width_a = sum(sizes[m] for m in members)
                piece = acts[:, :, start:start + width_a]
                if last is not None:
                    piece, last = lax.optimization_barrier((piece, last))
                cols = lax.all_to_all(piece, "node", split_axis=1, concat_axis=0, tiled=True)
                cols = cols.reshape(-1, width_a).T
                offset_a = 0
                for m in members:
                    columns[m] = cols[offset_a:offset_a + sizes[m]]
                    offset_a += sizes[m]
            cols, cot = columns[a], cots[b]
            if last is not None:
                cols, cot, last = lax.optimization_barrier((cols, cot, last))
            tok_group = cols.shape[1]
            rows = slice(start, start + size)
            grad = lax.dot_general(cols, cot, rows_by_tokens, preferred_element_type=jnp.float32)
            grad = grad / tok_group
            renewed = moment_decay * momentum[0, rows, span].astype(jnp.float32) + grad
            half = (params[0, rows, span].astype(jnp.float32) - rate * renewed).astype(jnp.bfloat16)
            last = half
            if weight_sent is None and b == 0 and a == len(sizes) - 1:
                weight, last = lax.optimization_barrier((push_weight, last))
                weight_sent = (shifted(weight, "grp", amount), shifted(weight, "grp", groups - amount))
            minus = shifted(half, "grp", amount)
            if paired:
                peers = (back_share * minus.astype(jnp.float32)) + front_share * minus.astype(jnp.float32)
            else:
                plus = shifted(half, "grp", groups - amount)
                peers = w_minus * minus.astype(jnp.float32) + w_plus * plus.astype(jnp.float32)
            total = keep_share * half.astype(jnp.float32) + peers
            mixed = lax.dynamic_update_slice(mixed, total.astype(jnp.bfloat16), (start, col_starts[b]))
    weight_minus, weight_plus = weight_sent
    new_weight = keep_share * push_weight + w_minus * weight_minus + w_plus * weight_plus
    return mixed[None], new_weight


def per_device(params, momentum, hidden, cotangent, push_weight, offsets, step):
    groups = lax.axis_size("grp")
    position = step[0]
    offset = offsets[position]
    rate = base_rate * (1.0 - 0.5 * position.astype(jnp.float32) / offsets.shape[0])
    amounts = list(range(1, groups // 2 + 1))
    direct = offset <= groups // 2
    index = jnp.where(direct, offset, groups - offset) - 1
    branches = [
        (lambda *a, amount=amount: pipeline(amount, groups, *a))
        for amount in amounts
    ]
    return lax.switch(
        index, branches, params, momentum, hidden[0], cotangent[0], push_weight, rate, direct
    )


def solution(mesh):
    in_specs = (
        P("grp", "node", None),
        P("grp", "node", None),
        P("grp", "node", None),
        P("grp", "node", None),
        P("grp"),
        P(),
        P(),
    )
    out_specs = (P("grp", "node", None), P("grp"))
    return jax.shard_map(
        per_device, mesh=mesh, in_specs=in_specs, out_specs=out_specs, check_vma=False
    )
```

```python
import jax
import jax.numpy as jnp
from jax import lax
from jax.sharding import PartitionSpec as P

base_rate = 40.0
moment_decay = 0.9
keep_share = 0.5
back_share = 0.3
front_share = 0.2
rows_by_tokens = (((1,), (0,)), ((), ()))
col_blocks = 4


def shifted(value, axis, steps):
    count = lax.axis_size(axis)
    pairs = [(source, (source + steps) % count) for source in range(count)]
    return lax.ppermute(value, axis, pairs)


def block_count(length, target, quantum):
    for count in range(target, 0, -1):
        if length % count == 0 and (length // count) % quantum == 0:
            return count
    return 1


def row_sizes(rows, quantum=16):
    sizes, size, left = [], 128, rows
    while left > 0:
        take = left if (left - size < size or size % quantum) else size
        sizes.append(take)
        left -= take
        if len(sizes) > 1:
            size *= 4 if len(sizes) == 2 else 2
    return sizes


def pipeline(amount, groups, params, momentum, hidden, cotangent, push_weight, rate, direct):
    nodes = lax.axis_size("node")
    rows_total = params.shape[1]
    acts = hidden.reshape(hidden.shape[0], nodes, rows_total)
    width = cotangent.shape[1]
    n_cols = block_count(width, col_blocks, 128)
    col_size = width // n_cols
    paired = (2 * amount) % groups == 0
    w_minus = jnp.where(direct, back_share, front_share).astype(jnp.float32)
    w_plus = jnp.where(direct, front_share, back_share).astype(jnp.float32)
    cots = [
        lax.all_gather(cotangent[:, b * col_size:(b + 1) * col_size], "node", axis=0, tiled=True)
        for b in range(n_cols)
    ]
    mixed = jnp.zeros(params.shape[1:], jnp.bfloat16)
    sizes = row_sizes(rows_total)
    starts = [sum(sizes[:i]) for i in range(len(sizes))]
    columns = [None] * len(sizes)
    weight_sent = None
    last = None
    for b in range(n_cols):
        span = slice(b * col_size, (b + 1) * col_size)
        for a, (start, size) in enumerate(zip(starts, sizes)):
            if columns[a] is None:
                members = [0, 1][:len(sizes)] if a == 0 else [a]
                width_a = sum(sizes[m] for m in members)
                piece = acts[:, :, start:start + width_a]
                if last is not None:
                    piece, last = lax.optimization_barrier((piece, last))
                cols = lax.all_to_all(piece, "node", split_axis=1, concat_axis=0, tiled=True)
                cols = cols.reshape(-1, width_a).T
                offset_a = 0
                for m in members:
                    columns[m] = cols[offset_a:offset_a + sizes[m]]
                    offset_a += sizes[m]
            cols, cot = columns[a], cots[b]
            if last is not None:
                cols, cot, last = lax.optimization_barrier((cols, cot, last))
            tok_group = cols.shape[1]
            rows = slice(start, start + size)
            grad = lax.dot_general(cols, cot, rows_by_tokens, preferred_element_type=jnp.float32)
            grad = grad / tok_group
            renewed = moment_decay * momentum[0, rows, span].astype(jnp.float32) + grad
            half = (params[0, rows, span].astype(jnp.float32) - rate * renewed).astype(jnp.bfloat16)
            last = half
            if weight_sent is None and b == 0 and a == len(sizes) - 1:
                weight, last = lax.optimization_barrier((push_weight, last))
                weight_sent = (shifted(weight, "grp", amount), shifted(weight, "grp", groups - amount))
            minus = shifted(half, "grp", amount)
            if paired:
                peers = (back_share * minus.astype(jnp.float32)) + front_share * minus.astype(jnp.float32)
            else:
                plus = shifted(half, "grp", groups - amount)
                peers = w_minus * minus.astype(jnp.float32) + w_plus * plus.astype(jnp.float32)
            total = keep_share * half.astype(jnp.float32) + peers
            mixed = lax.dynamic_update_slice(mixed, total.astype(jnp.bfloat16), (start, b * col_size))
    weight_minus, weight_plus = weight_sent
    new_weight = keep_share * push_weight + w_minus * weight_minus + w_plus * weight_plus
    return mixed[None], new_weight


def per_device(params, momentum, hidden, cotangent, push_weight, offsets, step):
    groups = lax.axis_size("grp")
    position = step[0]
    offset = offsets[position]
    rate = base_rate * (1.0 - 0.5 * position.astype(jnp.float32) / offsets.shape[0])
    amounts = list(range(1, groups // 2 + 1))
    direct = offset <= groups // 2
    index = jnp.where(direct, offset, groups - offset) - 1
    branches = [
        (lambda *a, amount=amount: pipeline(amount, groups, *a))
        for amount in amounts
    ]
    return lax.switch(
        index, branches, params, momentum, hidden[0], cotangent[0], push_weight, rate, direct
    )


def solution(mesh):
    in_specs = (
        P("grp", "node", None),
        P("grp", "node", None),
        P("grp", "node", None),
        P("grp", "node", None),
        P("grp"),
        P(),
        P(),
    )
    out_specs = (P("grp", "node", None), P("grp"))
    return jax.shard_map(
        per_device, mesh=mesh, in_specs=in_specs, out_specs=out_specs, check_vma=False
    )
```

```python
import jax
import jax.numpy as jnp
from jax import lax
from jax.sharding import PartitionSpec as P

base_rate = 40.0
moment_decay = 0.9
keep_share = 0.5
back_share = 0.3
front_share = 0.2
rows_by_tokens = (((1,), (0,)), ((), ()))
col_blocks = 4


def shifted(value, axis, steps):
    count = lax.axis_size(axis)
    pairs = [(source, (source + steps) % count) for source in range(count)]
    return lax.ppermute(value, axis, pairs)


def block_count(length, target, quantum):
    for count in range(target, 0, -1):
        if length % count == 0 and (length // count) % quantum == 0:
            return count
    return 1


def row_sizes(rows, quantum=16):
    sizes, size, left = [], 128, rows
    while left > 0:
        take = left if (left - size < size or size % quantum) else size
        sizes.append(take)
        left -= take
        size *= 2
    return sizes


def switched_sends(amount, groups, direct):
    paired = (2 * amount) % groups == 0
    w_minus = jnp.where(direct, back_share, front_share).astype(jnp.float32)
    w_plus = jnp.where(direct, front_share, back_share).astype(jnp.float32)

    def send_tile(half):
        minus = shifted(half, "grp", amount)
        if paired:
            return (back_share * minus.astype(jnp.float32)) + front_share * minus.astype(jnp.float32)
        plus = shifted(half, "grp", groups - amount)
        return w_minus * minus.astype(jnp.float32) + w_plus * plus.astype(jnp.float32)

    def send_weight(weight):
        return w_minus * shifted(weight, "grp", amount) + w_plus * shifted(weight, "grp", groups - amount)

    return send_tile, send_weight


def relayed_sends(groups, offset):
    far = offset * 2 == groups
    direct = offset == 1
    w_minus = jnp.where(direct, back_share, front_share).astype(jnp.float32)
    w_plus = jnp.where(direct, front_share, back_share).astype(jnp.float32)

    def send_tile(half):
        cut = half.shape[0] // 2
        top, bottom = half[:cut], half[cut:]
        up_1 = shifted(top, "grp", 1)
        down_1 = shifted(jnp.where(far, bottom, top), "grp", groups - 1)
        up_2 = shifted(jnp.where(far, up_1, bottom), "grp", 1)
        down_2 = shifted(jnp.where(far, down_1, bottom), "grp", groups - 1)
        minus = jnp.concatenate([up_1, up_2], axis=0).astype(jnp.float32)
        plus = jnp.concatenate([down_1, down_2], axis=0).astype(jnp.float32)
        other = jnp.concatenate([up_2, down_2], axis=0).astype(jnp.float32)
        near = w_minus * minus + w_plus * plus
        return jnp.where(far, back_share * other + front_share * other, near)

    def send_weight(weight):
        up_1 = shifted(weight, "grp", 1)
        down_1 = shifted(weight, "grp", groups - 1)
        up_2 = shifted(up_1, "grp", 1)
        near = w_minus * up_1 + w_plus * down_1
        return jnp.where(far, back_share * up_2 + front_share * up_2, near)

    return send_tile, send_weight


def pipeline(sends, params, momentum, hidden, cotangent, push_weight, rate):
    send_tile, send_weight = sends
    nodes = lax.axis_size("node")
    rows_total = params.shape[1]
    acts = hidden.reshape(hidden.shape[0], nodes, rows_total)
    width = cotangent.shape[1]
    n_cols = block_count(width, col_blocks, 128)
    col_size = width // n_cols
    cots = [
        lax.all_gather(cotangent[:, b * col_size:(b + 1) * col_size], "node", axis=0, tiled=True)
        for b in range(n_cols)
    ]
    mixed = jnp.zeros(params.shape[1:], jnp.bfloat16)
    sizes = row_sizes(rows_total)
    starts = [sum(sizes[:i]) for i in range(len(sizes))]
    columns = [None] * len(sizes)
    weight_sent = None
    last = None
    for b in range(n_cols):
        span = slice(b * col_size, (b + 1) * col_size)
        for a, (start, size) in enumerate(zip(starts, sizes)):
            if columns[a] is None:
                members = [0, 1][:len(sizes)] if a == 0 else [a]
                width_a = sum(sizes[m] for m in members)
                piece = acts[:, :, start:start + width_a]
                if last is not None:
                    piece, last = lax.optimization_barrier((piece, last))
                cols = lax.all_to_all(piece, "node", split_axis=1, concat_axis=0, tiled=True)
                cols = cols.reshape(-1, width_a).T
                offset_a = 0
                for m in members:
                    columns[m] = cols[offset_a:offset_a + sizes[m]]
                    offset_a += sizes[m]
            cols, cot = columns[a], cots[b]
            if last is not None:
                cols, cot, last = lax.optimization_barrier((cols, cot, last))
            tok_group = cols.shape[1]
            rows = slice(start, start + size)
            grad = lax.dot_general(cols, cot, rows_by_tokens, preferred_element_type=jnp.float32)
            grad = grad / tok_group
            renewed = moment_decay * momentum[0, rows, span].astype(jnp.float32) + grad
            half = (params[0, rows, span].astype(jnp.float32) - rate * renewed).astype(jnp.bfloat16)
            last = half
            if weight_sent is None and b == 0 and a == len(sizes) - 1:
                weight, last = lax.optimization_barrier((push_weight, last))
                weight_sent = send_weight(weight)
            peers = send_tile(half)
            total = keep_share * half.astype(jnp.float32) + peers
            mixed = lax.dynamic_update_slice(mixed, total.astype(jnp.bfloat16), (start, b * col_size))
    new_weight = keep_share * push_weight + weight_sent
    return mixed[None], new_weight


def per_device(params, momentum, hidden, cotangent, push_weight, offsets, step):
    groups = lax.axis_size("grp")
    position = step[0]
    offset = offsets[position]
    rate = base_rate * (1.0 - 0.5 * position.astype(jnp.float32) / offsets.shape[0])
    args = (params, momentum, hidden[0], cotangent[0], push_weight, rate)
    if groups == 4:
        return pipeline(relayed_sends(groups, offset), *args)
    amounts = list(range(1, groups // 2 + 1))
    direct = offset <= groups // 2
    index = jnp.where(direct, offset, groups - offset) - 1
    branches = [
        (lambda *a, amount=amount: pipeline(switched_sends(amount, groups, direct), *a))
        for amount in amounts
    ]
    return lax.switch(index, branches, *args)


def solution(mesh):
    in_specs = (
        P("grp", "node", None),
        P("grp", "node", None),
        P("grp", "node", None),
        P("grp", "node", None),
        P("grp"),
        P(),
        P(),
    )
    out_specs = (P("grp", "node", None), P("grp"))
    return jax.shard_map(
        per_device, mesh=mesh, in_specs=in_specs, out_specs=out_specs, check_vma=False
    )
```

```python
import jax
import jax.numpy as jnp
from jax import lax
from jax.sharding import PartitionSpec as P

base_rate = 40.0
moment_decay = 0.9
keep_share = 0.5
back_share = 0.3
front_share = 0.2
rows_by_tokens = (((1,), (0,)), ((), ()))
col_blocks = 4


def shifted(value, axis, steps):
    count = lax.axis_size(axis)
    pairs = [(source, (source + steps) % count) for source in range(count)]
    return lax.ppermute(value, axis, pairs)


def block_count(length, target, quantum):
    for count in range(target, 0, -1):
        if length % count == 0 and (length // count) % quantum == 0:
            return count
    return 1


def row_sizes(rows, quantum=16):
    sizes, size, left = [], 128, rows
    while left > 0:
        take = left if (left - size < size or size % quantum) else size
        sizes.append(take)
        left -= take
        size *= 2
    return sizes


def pipeline(amount, groups, params, momentum, hidden, cotangent, push_weight, rate, direct):
    nodes = lax.axis_size("node")
    rows_total = params.shape[1]
    acts = hidden.reshape(hidden.shape[0], nodes, rows_total)
    width = cotangent.shape[1]
    n_cols = block_count(width, col_blocks, 128)
    col_size = width // n_cols
    paired = (2 * amount) % groups == 0
    w_minus = jnp.where(direct, back_share, front_share).astype(jnp.float32)
    w_plus = jnp.where(direct, front_share, back_share).astype(jnp.float32)
    cots = [
        lax.all_gather(cotangent[:, b * col_size:(b + 1) * col_size], "node", axis=0, tiled=True)
        for b in range(n_cols)
    ]
    mixed = jnp.zeros(params.shape[1:], jnp.bfloat16)
    sizes = row_sizes(rows_total)
    starts = [sum(sizes[:i]) for i in range(len(sizes))]
    columns = [None] * len(sizes)
    weight_sent = None
    first_total = None
    last = None
    for b in range(n_cols):
        span = slice(b * col_size, (b + 1) * col_size)
        for a, (start, size) in enumerate(zip(starts, sizes)):
            if columns[a] is None:
                members = [0, 1][:len(sizes)] if a == 0 else [a]
                width_a = sum(sizes[m] for m in members)
                piece = acts[:, :, start:start + width_a]
                if last is not None and first_total is not None:
                    piece, last, first_total = lax.optimization_barrier((piece, last, first_total))
                elif last is not None:
                    piece, last = lax.optimization_barrier((piece, last))
                cols = lax.all_to_all(piece, "node", split_axis=1, concat_axis=0, tiled=True)
                cols = cols.reshape(-1, width_a).T
                offset_a = 0
                for m in members:
                    columns[m] = cols[offset_a:offset_a + sizes[m]]
                    offset_a += sizes[m]
            cols, cot = columns[a], cots[b]
            if last is not None:
                cols, cot, last = lax.optimization_barrier((cols, cot, last))
            tok_group = cols.shape[1]
            rows = slice(start, start + size)
            grad = lax.dot_general(cols, cot, rows_by_tokens, preferred_element_type=jnp.float32)
            grad = grad / tok_group
            renewed = moment_decay * momentum[0, rows, span].astype(jnp.float32) + grad
            half = (params[0, rows, span].astype(jnp.float32) - rate * renewed).astype(jnp.bfloat16)
            last = half
            if weight_sent is None and b == 0 and a == len(sizes) - 1:
                weight, last = lax.optimization_barrier((push_weight, last))
                weight_sent = (shifted(weight, "grp", amount), shifted(weight, "grp", groups - amount))
            minus = shifted(half, "grp", amount)
            if paired:
                peers = (back_share * minus.astype(jnp.float32)) + front_share * minus.astype(jnp.float32)
            else:
                plus = shifted(half, "grp", groups - amount)
                peers = w_minus * minus.astype(jnp.float32) + w_plus * plus.astype(jnp.float32)
            total = keep_share * half.astype(jnp.float32) + peers
            if first_total is None:
                first_total = total
            mixed = lax.dynamic_update_slice(mixed, total.astype(jnp.bfloat16), (start, b * col_size))
    weight_minus, weight_plus = weight_sent
    new_weight = keep_share * push_weight + w_minus * weight_minus + w_plus * weight_plus
    return mixed[None], new_weight


def per_device(params, momentum, hidden, cotangent, push_weight, offsets, step):
    groups = lax.axis_size("grp")
    position = step[0]
    offset = offsets[position]
    rate = base_rate * (1.0 - 0.5 * position.astype(jnp.float32) / offsets.shape[0])
    amounts = list(range(1, groups // 2 + 1))
    direct = offset <= groups // 2
    index = jnp.where(direct, offset, groups - offset) - 1
    branches = [
        (lambda *a, amount=amount: pipeline(amount, groups, *a))
        for amount in amounts
    ]
    return lax.switch(
        index, branches, params, momentum, hidden[0], cotangent[0], push_weight, rate, direct
    )


def solution(mesh):
    in_specs = (
        P("grp", "node", None),
        P("grp", "node", None),
        P("grp", "node", None),
        P("grp", "node", None),
        P("grp"),
        P(),
        P(),
    )
    out_specs = (P("grp", "node", None), P("grp"))
    return jax.shard_map(
        per_device, mesh=mesh, in_specs=in_specs, out_specs=out_specs, check_vma=False
    )
```

```python
import jax
import jax.numpy as jnp
from jax import lax
from jax.sharding import PartitionSpec as P

base_rate = 40.0
moment_decay = 0.9
keep_share = 0.5
back_share = 0.3
front_share = 0.2
rows_by_tokens = (((1,), (0,)), ((), ()))
col_blocks = 4


def shifted(value, axis, steps):
    count = lax.axis_size(axis)
    pairs = [(source, (source + steps) % count) for source in range(count)]
    return lax.ppermute(value, axis, pairs)


def block_count(length, target, quantum):
    for count in range(target, 0, -1):
        if length % count == 0 and (length // count) % quantum == 0:
            return count
    return 1


def row_sizes(rows, quantum=16):
    sizes, size, left = [], 128, rows
    while left > 0:
        take = left if (left - size < size or size % quantum) else size
        sizes.append(take)
        left -= take
        size *= 2
    return sizes


def half_step(cols, cot, params, momentum, rate):
    tok_group = cols.shape[1]
    grad = lax.dot_general(cols, cot, rows_by_tokens, preferred_element_type=jnp.float32)
    grad = grad / tok_group
    renewed = moment_decay * momentum.astype(jnp.float32) + grad
    return (params.astype(jnp.float32) - rate * renewed).astype(jnp.bfloat16)


def head_tiles(params, momentum, hidden, cotangent, rate):
    nodes = lax.axis_size("node")
    rows_total = params.shape[1]
    acts = hidden.reshape(hidden.shape[0], nodes, rows_total)
    col_size = cotangent.shape[1] // block_count(cotangent.shape[1], col_blocks, 128)
    sizes = row_sizes(rows_total)[:2]
    width_a = sum(sizes)
    first_cots = lax.all_gather(cotangent[:, :col_size], "node", axis=0, tiled=True)
    cols = lax.all_to_all(acts[:, :, :width_a], "node", split_axis=1, concat_axis=0, tiled=True)
    cols = cols.reshape(-1, width_a).T
    columns, halves, start = [], [], 0
    for size in sizes:
        columns.append(cols[start:start + size])
        rows = slice(start, start + size)
        halves.append(
            half_step(columns[-1], first_cots, params[0, rows, :col_size], momentum[0, rows, :col_size], rate)
        )
        start += size
    return first_cots, tuple(columns), tuple(halves)


def pipeline(amount, groups, params, momentum, hidden, cotangent, push_weight, rate, direct, head):
    nodes = lax.axis_size("node")
    rows_total = params.shape[1]
    acts = hidden.reshape(hidden.shape[0], nodes, rows_total)
    width = cotangent.shape[1]
    n_cols = block_count(width, col_blocks, 128)
    col_size = width // n_cols
    paired = (2 * amount) % groups == 0
    w_minus = jnp.where(direct, back_share, front_share).astype(jnp.float32)
    w_plus = jnp.where(direct, front_share, back_share).astype(jnp.float32)
    first_cots, first_columns, first_halves = head
    cots = [first_cots] + [
        lax.all_gather(cotangent[:, b * col_size:(b + 1) * col_size], "node", axis=0, tiled=True)
        for b in range(1, n_cols)
    ]
    mixed = jnp.zeros(params.shape[1:], jnp.bfloat16)
    sizes = row_sizes(rows_total)
    starts = [sum(sizes[:i]) for i in range(len(sizes))]
    columns = list(first_columns) + [None] * (len(sizes) - len(first_columns))
    weight_sent = None
    last = None
    for b in range(n_cols):
        span = slice(b * col_size, (b + 1) * col_size)
        for a, (start, size) in enumerate(zip(starts, sizes)):
            if columns[a] is None:
                members = [0, 1][:len(sizes)] if a == 0 else [a]
                width_a = sum(sizes[m] for m in members)
                piece = acts[:, :, start:start + width_a]
                if last is not None:
                    piece, last = lax.optimization_barrier((piece, last))
                cols = lax.all_to_all(piece, "node", split_axis=1, concat_axis=0, tiled=True)
                cols = cols.reshape(-1, width_a).T
                offset_a = 0
                for m in members:
                    columns[m] = cols[offset_a:offset_a + sizes[m]]
                    offset_a += sizes[m]
            rows = slice(start, start + size)
            if b == 0 and a < len(first_halves):
                half = first_halves[a]
            else:
                cols, cot = columns[a], cots[b]
                if last is not None:
                    cols, cot, last = lax.optimization_barrier((cols, cot, last))
                half = half_step(cols, cot, params[0, rows, span], momentum[0, rows, span], rate)
            last = half
            if weight_sent is None and b == 0 and a == len(sizes) - 1:
                weight, last = lax.optimization_barrier((push_weight, last))
                weight_sent = (shifted(weight, "grp", amount), shifted(weight, "grp", groups - amount))
            minus = shifted(half, "grp", amount)
            if paired:
                peers = (back_share * minus.astype(jnp.float32)) + front_share * minus.astype(jnp.float32)
            else:
                plus = shifted(half, "grp", groups - amount)
                peers = w_minus * minus.astype(jnp.float32) + w_plus * plus.astype(jnp.float32)
            total = keep_share * half.astype(jnp.float32) + peers
            mixed = lax.dynamic_update_slice(mixed, total.astype(jnp.bfloat16), (start, b * col_size))
    weight_minus, weight_plus = weight_sent
    new_weight = keep_share * push_weight + w_minus * weight_minus + w_plus * weight_plus
    return mixed[None], new_weight


def per_device(params, momentum, hidden, cotangent, push_weight, offsets, step):
    groups = lax.axis_size("grp")
    position = step[0]
    offset = offsets[position]
    rate = base_rate * (1.0 - 0.5 * position.astype(jnp.float32) / offsets.shape[0])
    amounts = list(range(1, groups // 2 + 1))
    direct = offset <= groups // 2
    index = jnp.where(direct, offset, groups - offset) - 1
    branches = [
        (lambda *a, amount=amount: pipeline(amount, groups, *a))
        for amount in amounts
    ]
    head = head_tiles(params, momentum, hidden[0], cotangent[0], rate)
    return lax.switch(
        index, branches, params, momentum, hidden[0], cotangent[0], push_weight, rate, direct, head
    )


def solution(mesh):
    in_specs = (
        P("grp", "node", None),
        P("grp", "node", None),
        P("grp", "node", None),
        P("grp", "node", None),
        P("grp"),
        P(),
        P(),
    )
    out_specs = (P("grp", "node", None), P("grp"))
    return jax.shard_map(
        per_device, mesh=mesh, in_specs=in_specs, out_specs=out_specs, check_vma=False
    )
```

```python
import jax
import jax.numpy as jnp
from jax import lax
from jax.sharding import PartitionSpec as P

base_rate = 40.0
moment_decay = 0.9
keep_share = 0.5
back_share = 0.3
front_share = 0.2
rows_by_tokens = (((1,), (0,)), ((), ()))
col_blocks = 4


def shifted(value, axis, steps):
    count = lax.axis_size(axis)
    pairs = [(source, (source + steps) % count) for source in range(count)]
    return lax.ppermute(value, axis, pairs)


def block_count(length, target, quantum):
    for count in range(target, 0, -1):
        if length % count == 0 and (length // count) % quantum == 0:
            return count
    return 1


def row_sizes(rows, quantum=16):
    sizes, size, left = [], 128, rows
    while left > 0:
        take = left if (left - size < size or size % quantum) else size
        sizes.append(take)
        left -= take
        size *= 2
    return sizes


def column_sizes(width):
    quarter = width // col_blocks
    if width % col_blocks or quarter % 256:
        count = block_count(width, col_blocks, 128)
        return [width // count] * count
    return [quarter // 2, quarter // 2] + [quarter] * (col_blocks - 1)


def pipeline(amount, groups, params, momentum, hidden, cotangent, push_weight, rate, direct):
    nodes = lax.axis_size("node")
    rows_total = params.shape[1]
    acts = hidden.reshape(hidden.shape[0], nodes, rows_total)
    width = cotangent.shape[1]
    col_sizes = column_sizes(width)
    n_cols = len(col_sizes)
    col_starts = [sum(col_sizes[:i]) for i in range(n_cols)]
    paired = (2 * amount) % groups == 0
    w_minus = jnp.where(direct, back_share, front_share).astype(jnp.float32)
    w_plus = jnp.where(direct, front_share, back_share).astype(jnp.float32)
    cots = [
        lax.all_gather(cotangent[:, lo:lo + size], "node", axis=0, tiled=True)
        for lo, size in zip(col_starts, col_sizes)
    ]
    mixed = jnp.zeros(params.shape[1:], jnp.bfloat16)
    sizes = row_sizes(rows_total)
    starts = [sum(sizes[:i]) for i in range(len(sizes))]
    columns = [None] * len(sizes)
    weight_sent = None
    last = None
    for b in range(n_cols):
        span = slice(col_starts[b], col_starts[b] + col_sizes[b])
        for a, (start, size) in enumerate(zip(starts, sizes)):
            if columns[a] is None:
                members = [0, 1][:len(sizes)] if a == 0 else [a]
                width_a = sum(sizes[m] for m in members)
                piece = acts[:, :, start:start + width_a]
                if last is not None:
                    piece, last = lax.optimization_barrier((piece, last))
                cols = lax.all_to_all(piece, "node", split_axis=1, concat_axis=0, tiled=True)
                cols = cols.reshape(-1, width_a).T
                offset_a = 0
                for m in members:
                    columns[m] = cols[offset_a:offset_a + sizes[m]]
                    offset_a += sizes[m]
            cols, cot = columns[a], cots[b]
            if last is not None:
                cols, cot, last = lax.optimization_barrier((cols, cot, last))
            tok_group = cols.shape[1]
            rows = slice(start, start + size)
            grad = lax.dot_general(cols, cot, rows_by_tokens, preferred_element_type=jnp.float32)
            grad = grad / tok_group
            renewed = moment_decay * momentum[0, rows, span].astype(jnp.float32) + grad
            half = (params[0, rows, span].astype(jnp.float32) - rate * renewed).astype(jnp.bfloat16)
            last = half
            if weight_sent is None and b == 0 and a == len(sizes) - 1:
                weight, last = lax.optimization_barrier((push_weight, last))
                weight_sent = (shifted(weight, "grp", amount), shifted(weight, "grp", groups - amount))
            minus = shifted(half, "grp", amount)
            if paired:
                peers = (back_share * minus.astype(jnp.float32)) + front_share * minus.astype(jnp.float32)
            else:
                plus = shifted(half, "grp", groups - amount)
                peers = w_minus * minus.astype(jnp.float32) + w_plus * plus.astype(jnp.float32)
            total = keep_share * half.astype(jnp.float32) + peers
            mixed = lax.dynamic_update_slice(mixed, total.astype(jnp.bfloat16), (start, col_starts[b]))
    weight_minus, weight_plus = weight_sent
    new_weight = keep_share * push_weight + w_minus * weight_minus + w_plus * weight_plus
    return mixed[None], new_weight


def per_device(params, momentum, hidden, cotangent, push_weight, offsets, step):
    groups = lax.axis_size("grp")
    position = step[0]
    offset = offsets[position]
    rate = base_rate * (1.0 - 0.5 * position.astype(jnp.float32) / offsets.shape[0])
    amounts = list(range(1, groups // 2 + 1))
    direct = offset <= groups // 2
    index = jnp.where(direct, offset, groups - offset) - 1
    branches = [
        (lambda *a, amount=amount: pipeline(amount, groups, *a))
        for amount in amounts
    ]
    return lax.switch(
        index, branches, params, momentum, hidden[0], cotangent[0], push_weight, rate, direct
    )


def solution(mesh):
    in_specs = (
        P("grp", "node", None),
        P("grp", "node", None),
        P("grp", "node", None),
        P("grp", "node", None),
        P("grp"),
        P(),
        P(),
    )
    out_specs = (P("grp", "node", None), P("grp"))
    return jax.shard_map(
        per_device, mesh=mesh, in_specs=in_specs, out_specs=out_specs, check_vma=False
    )
```

```python
import jax
import jax.numpy as jnp
from jax import lax
from jax.sharding import PartitionSpec as P

base_rate = 40.0
moment_decay = 0.9
keep_share = 0.5
back_share = 0.3
front_share = 0.2
rows_by_tokens = (((1,), (0,)), ((), ()))
col_blocks = 4


def shifted(value, axis, steps):
    count = lax.axis_size(axis)
    pairs = [(source, (source + steps) % count) for source in range(count)]
    return lax.ppermute(value, axis, pairs)


def block_count(length, target, quantum):
    for count in range(target, 0, -1):
        if length % count == 0 and (length // count) % quantum == 0:
            return count
    return 1


def row_sizes(rows, quantum=16):
    sizes, size, left = [], 128, rows
    while left > 0:
        take = left if (left - size < size or size % quantum) else size
        sizes.append(take)
        left -= take
        size *= 2
    return sizes


def pipeline(amount, groups, params, momentum, hidden, cotangent, push_weight, rate, direct):
    nodes = lax.axis_size("node")
    rows_total = params.shape[1]
    acts = hidden.reshape(hidden.shape[0], nodes, rows_total)
    width = cotangent.shape[1]
    n_cols = block_count(width, col_blocks, 128)
    col_size = width // n_cols
    paired = (2 * amount) % groups == 0
    w_minus = jnp.where(direct, back_share, front_share).astype(jnp.float32)
    w_plus = jnp.where(direct, front_share, back_share).astype(jnp.float32)
    first = lax.all_gather(cotangent[:, :col_size], "node", axis=0, tiled=True)
    cots = [first]
    if n_cols > 1:
        rest = lax.all_gather(cotangent[:, col_size:], "node", axis=0, tiled=True)
        cots += [rest[:, (b - 1) * col_size:b * col_size] for b in range(1, n_cols)]
    mixed = jnp.zeros(params.shape[1:], jnp.bfloat16)
    sizes = row_sizes(rows_total)
    starts = [sum(sizes[:i]) for i in range(len(sizes))]
    columns = [None] * len(sizes)
    weight_sent = None
    last = None
    for b in range(n_cols):
        span = slice(b * col_size, (b + 1) * col_size)
        for a, (start, size) in enumerate(zip(starts, sizes)):
            if columns[a] is None:
                members = [0, 1][:len(sizes)] if a == 0 else [a]
                width_a = sum(sizes[m] for m in members)
                piece = acts[:, :, start:start + width_a]
                if last is not None:
                    piece, last = lax.optimization_barrier((piece, last))
                cols = lax.all_to_all(piece, "node", split_axis=1, concat_axis=0, tiled=True)
                cols = cols.reshape(-1, width_a).T
                offset_a = 0
                for m in members:
                    columns[m] = cols[offset_a:offset_a + sizes[m]]
                    offset_a += sizes[m]
            cols, cot = columns[a], cots[b]
            if last is not None:
                cols, cot, last = lax.optimization_barrier((cols, cot, last))
            tok_group = cols.shape[1]
            rows = slice(start, start + size)
            grad = lax.dot_general(cols, cot, rows_by_tokens, preferred_element_type=jnp.float32)
            grad = grad / tok_group
            renewed = moment_decay * momentum[0, rows, span].astype(jnp.float32) + grad
            half = (params[0, rows, span].astype(jnp.float32) - rate * renewed).astype(jnp.bfloat16)
            last = half
            if weight_sent is None and b == 0 and a == len(sizes) - 1:
                weight, last = lax.optimization_barrier((push_weight, last))
                weight_sent = (shifted(weight, "grp", amount), shifted(weight, "grp", groups - amount))
            minus = shifted(half, "grp", amount)
            if paired:
                peers = (back_share * minus.astype(jnp.float32)) + front_share * minus.astype(jnp.float32)
            else:
                plus = shifted(half, "grp", groups - amount)
                peers = w_minus * minus.astype(jnp.float32) + w_plus * plus.astype(jnp.float32)
            total = keep_share * half.astype(jnp.float32) + peers
            mixed = lax.dynamic_update_slice(mixed, total.astype(jnp.bfloat16), (start, b * col_size))
    weight_minus, weight_plus = weight_sent
    new_weight = keep_share * push_weight + w_minus * weight_minus + w_plus * weight_plus
    return mixed[None], new_weight


def per_device(params, momentum, hidden, cotangent, push_weight, offsets, step):
    groups = lax.axis_size("grp")
    position = step[0]
    offset = offsets[position]
    rate = base_rate * (1.0 - 0.5 * position.astype(jnp.float32) / offsets.shape[0])
    amounts = list(range(1, groups // 2 + 1))
    direct = offset <= groups // 2
    index = jnp.where(direct, offset, groups - offset) - 1
    branches = [
        (lambda *a, amount=amount: pipeline(amount, groups, *a))
        for amount in amounts
    ]
    return lax.switch(
        index, branches, params, momentum, hidden[0], cotangent[0], push_weight, rate, direct
    )


def solution(mesh):
    in_specs = (
        P("grp", "node", None),
        P("grp", "node", None),
        P("grp", "node", None),
        P("grp", "node", None),
        P("grp"),
        P(),
        P(),
    )
    out_specs = (P("grp", "node", None), P("grp"))
    return jax.shard_map(
        per_device, mesh=mesh, in_specs=in_specs, out_specs=out_specs, check_vma=False
    )
```

```python
import jax
import jax.numpy as jnp
from jax import lax
from jax.sharding import PartitionSpec as P

base_rate = 40.0
moment_decay = 0.9
keep_share = 0.5
back_share = 0.3
front_share = 0.2
rows_by_tokens = (((1,), (0,)), ((), ()))
col_blocks = 4


def shifted(value, axis, steps):
    count = lax.axis_size(axis)
    pairs = [(source, (source + steps) % count) for source in range(count)]
    return lax.ppermute(value, axis, pairs)


def block_count(length, target, quantum):
    for count in range(target, 0, -1):
        if length % count == 0 and (length // count) % quantum == 0:
            return count
    return 1


def row_sizes(rows, quantum=16):
    sizes, size, left = [], 128, rows
    while left > 0:
        take = left if (left - size < size or size % quantum) else size
        sizes.append(take)
        left -= take
        size *= 2
    return sizes


def pipeline(amount, groups, params, momentum, hidden, cotangent, push_weight, rate, direct):
    nodes = lax.axis_size("node")
    rows_total = params.shape[1]
    acts = hidden.reshape(hidden.shape[0], nodes, rows_total)
    width = cotangent.shape[1]
    n_cols = block_count(width, col_blocks, 128)
    col_size = width // n_cols
    paired = (2 * amount) % groups == 0
    w_minus = jnp.where(direct, back_share, front_share).astype(jnp.float32)
    w_plus = jnp.where(direct, front_share, back_share).astype(jnp.float32)
    cots = [
        lax.all_gather(cotangent[:, b * col_size:(b + 1) * col_size], "node", axis=0, tiled=True)
        for b in range(n_cols)
    ]
    mixed = jnp.zeros(params.shape[1:], jnp.bfloat16)
    sizes = row_sizes(rows_total)
    starts = [sum(sizes[:i]) for i in range(len(sizes))]
    columns = [None] * len(sizes)
    weight_sent = None
    last = None
    for b in range(n_cols):
        span = slice(b * col_size, (b + 1) * col_size)
        order = list(range(len(sizes)))
        if b == n_cols - 1 and b > 0:
            order.reverse()
        for a in order:
            start, size = starts[a], sizes[a]
            if columns[a] is None:
                members = [0, 1][:len(sizes)] if a == 0 else [a]
                width_a = sum(sizes[m] for m in members)
                piece = acts[:, :, start:start + width_a]
                if last is not None:
                    piece, last = lax.optimization_barrier((piece, last))
                cols = lax.all_to_all(piece, "node", split_axis=1, concat_axis=0, tiled=True)
                cols = cols.reshape(-1, width_a).T
                offset_a = 0
                for m in members:
                    columns[m] = cols[offset_a:offset_a + sizes[m]]
                    offset_a += sizes[m]
            cols, cot = columns[a], cots[b]
            if last is not None:
                cols, cot, last = lax.optimization_barrier((cols, cot, last))
            tok_group = cols.shape[1]
            rows = slice(start, start + size)
            grad = lax.dot_general(cols, cot, rows_by_tokens, preferred_element_type=jnp.float32)
            grad = grad / tok_group
            renewed = moment_decay * momentum[0, rows, span].astype(jnp.float32) + grad
            half = (params[0, rows, span].astype(jnp.float32) - rate * renewed).astype(jnp.bfloat16)
            last = half
            if weight_sent is None and b == 0 and a == len(sizes) - 1:
                weight, last = lax.optimization_barrier((push_weight, last))
                weight_sent = (shifted(weight, "grp", amount), shifted(weight, "grp", groups - amount))
            minus = shifted(half, "grp", amount)
            if paired:
                peers = (back_share * minus.astype(jnp.float32)) + front_share * minus.astype(jnp.float32)
            else:
                plus = shifted(half, "grp", groups - amount)
                peers = w_minus * minus.astype(jnp.float32) + w_plus * plus.astype(jnp.float32)
            total = keep_share * half.astype(jnp.float32) + peers
            mixed = lax.dynamic_update_slice(mixed, total.astype(jnp.bfloat16), (start, b * col_size))
    weight_minus, weight_plus = weight_sent
    new_weight = keep_share * push_weight + w_minus * weight_minus + w_plus * weight_plus
    return mixed[None], new_weight


def per_device(params, momentum, hidden, cotangent, push_weight, offsets, step):
    groups = lax.axis_size("grp")
    position = step[0]
    offset = offsets[position]
    rate = base_rate * (1.0 - 0.5 * position.astype(jnp.float32) / offsets.shape[0])
    amounts = list(range(1, groups // 2 + 1))
    direct = offset <= groups // 2
    index = jnp.where(direct, offset, groups - offset) - 1
    branches = [
        (lambda *a, amount=amount: pipeline(amount, groups, *a))
        for amount in amounts
    ]
    return lax.switch(
        index, branches, params, momentum, hidden[0], cotangent[0], push_weight, rate, direct
    )


def solution(mesh):
    in_specs = (
        P("grp", "node", None),
        P("grp", "node", None),
        P("grp", "node", None),
        P("grp", "node", None),
        P("grp"),
        P(),
        P(),
    )
    out_specs = (P("grp", "node", None), P("grp"))
    return jax.shard_map(
        per_device, mesh=mesh, in_specs=in_specs, out_specs=out_specs, check_vma=False
    )
```
